256 devices in a mesh: dp: 8 (over z), expert: 32 (over y, x, core).
Axes of the slice: x: 4, y: 4, z: 8, core: 2. Of those that a mesh axis runs over, the one named last changes fastest.
Arguments:
- tokens: bfloat16 [32, 64, 4096], P('expert'), may hold values from -6 to 6
- norm_gain: float32 [4096], replicated, may hold values from 0.25 to 1.75
- expert_ids: int32 [32, 64, 8], P('expert'), may hold values from 0 to 63, all different within a row; in each aligned block of 64 rows (0 to 63, 64 to 127, ..., all dimensions but the last counted through in order) at most 16 rows name the same one
- route_weights: float32 [32, 64, 8], P('expert'), may hold values from 0.02 to 0.4
- gate_proj: bfloat16 [64, 1536, 4096], P('expert', 'dp'), may hold values from -0.09375 to 0.09375
- up_proj: bfloat16 [64, 1536, 4096], P('expert', 'dp'), may hold values from -0.09375 to 0.09375
- down_proj: bfloat16 [64, 1536, 4096], P('expert', 'dp'), may hold values from -0.15625 to 0.15625
Outputs:
- mixed: bfloat16 [32, 64, 4096], P('expert', 'dp')
The draws below stay inside these ranges and needn't reach their ends.
Inputs may be any that keep to these rules, and one draw needn't show every extreme that they name: `expert_ids`: each token names 8 different experts. Within one group no expert is named by more than 16 tokens, and in every draw some expert is named by exactly 16 tokens of some group.
All inputs are finite; a program needn't handle non-finite values.
Results may differ from the reference program's by a relative error of at most 0.019.
Values may be sent and summed in bfloat16 or wider, within the bound.
No kernel may reach another device: no remote copies, remote signals or barrier semaphores. Data moves between devices by JAX's collectives and lax.ppermute only.
A program may use at most 128 MiB of HBM per device.

```python
import math
import jax
import jax.numpy as jnp
import numpy as np
from jax import lax

D = 4096
FF = 1536
TOP = 8
GROUP_TOK = 64
EXPERTS = 64
GROUPS = 32
FF_DEV = 192
MOST = 16


def steps_of(key, extent, shards, low, largest):
    def one(axis_at, shards_of):
        steps = jax.random.uniform(jax.random.fold_in(jax.random.fold_in(key, 6), axis_at), (shards_of,), jnp.float32, low / len(shards), largest / len(shards))
        return jnp.repeat(jnp.exp(steps), extent[axis_at] // shards_of).reshape((-1,) + (1,) * (len(extent) - axis_at - 1))

    loudness = one(*shards[0])
    for cut in shards[1:]:
        loudness = loudness * one(*cut)
    return loudness


def assign_block(rng, own, number, rows, count, top, reach, skew):
    ranking = jax.random.permutation(rng, count)
    heavy_load, common = shares(count, rows * top, reach, skew, True), shares(count, rows * top, reach, skew, False)
    places = jnp.arange(count)

    def named(sizes, rotation):
        used = int((sizes > 0).sum())
        fixed = max(1, used // 4)
        passed = fixed + (places - fixed + rotation * (used - fixed)) % max(1, count - fixed)
        return jnp.zeros((count,), jnp.int32).at[ranking[jnp.where(places < fixed, places, passed)]].set(jnp.asarray(sizes, jnp.int32))

    sizes = jnp.where(number % 4 == 0, named(heavy_load, number // 4), named(common, number - number // 4 - 1))
    mixed = jax.random.permutation(jax.random.fold_in(own, 3), count)
    giver, taker = mixed[0:count // 2 * 2:2], mixed[1:count // 2 * 2:2]
    room = jnp.minimum(sizes[giver] - 1, reach - sizes[taker]) // 2
    room = jnp.where((giver == ranking[0]) | (taker == ranking[0]) | (sizes[taker] == 0), 0, jnp.maximum(room, 0))
    passed = jax.random.randint(jax.random.fold_in(own, 4), (count // 2,), 0, 1 << 20) % (room + 1)
    sizes = sizes.at[giver].add(-passed).at[taker].add(passed)
    members = jnp.searchsorted(jnp.cumsum(sizes), jnp.arange(rows * top), side="right").astype(jnp.int32)
    listing = members.reshape(top, rows).T
    listing = listing[jax.random.permutation(jax.random.fold_in(own, 1), rows)]
    rotation = jax.random.randint(jax.random.fold_in(own, 2), (rows, 1), 0, top)
    return jnp.take_along_axis(listing, (jnp.arange(top)[None, :] + rotation) % top, axis=1)


def shares(number_of, total, reach, lean, full):
    loads = [(1 << 20) // math.isqrt(grade ** lean) + 1 for grade in range(1, number_of + 1)]
    largest = reach if full else min(reach, max(-(-total // number_of), total * loads[0] // sum(loads)))
    least = 1 if total - largest >= number_of - 1 else 0
    holding, spare = [largest] + [least] * (number_of - 1), total - largest - least * (number_of - 1)
    while spare > 0:
        movable = [i for i in range(1, number_of) if holding[i] < largest] or [i for i in range(1, number_of) if holding[i] < reach]
        mass, left = sum([loads[i] for i in movable]), spare
        for i in movable:
            extra = min(reach - holding[i], max(1, left * loads[i] // mass), spare)
            holding[i] = holding[i] + extra
            spare = spare - extra
    return np.array(holding)


def gaussian(rng, dims, width, most, shards=(), kind=jnp.bfloat16):
    result = jax.random.normal(rng, dims, jnp.float32) * width
    if len(shards) > 0:
        result = steps_of(rng, dims, shards, -0.22, 0.18) * result
    return jnp.clip(result, min=-most, max=most).astype(kind)


def setup_inputs(seed: int = 0) -> dict:
    arg_keys = jax.random.split(jax.random.key(seed), 8)
    tokens = gaussian(arg_keys[0], (GROUPS, GROUP_TOK, D), 1.0, 6.0, ((0, 32),))
    norm_gain = jnp.clip(1.0 + 0.15 * jax.random.normal(arg_keys[1], (D,), jnp.float32), 0.25, 1.75)
    expert_ids_keys = jax.random.split(jax.random.fold_in(arg_keys[2], 1), GROUPS * GROUP_TOK // GROUP_TOK)
    expert_ids_turns = jax.random.permutation(jax.random.fold_in(arg_keys[2], 3), GROUPS * GROUP_TOK // GROUP_TOK)
    expert_ids = jax.vmap(lambda own, number: assign_block(jax.random.fold_in(arg_keys[2], 2), own, number, GROUP_TOK, EXPERTS, TOP, MOST, 2))(expert_ids_keys, expert_ids_turns).reshape((GROUPS, GROUP_TOK, TOP))
    route_weights = jnp.clip(jnp.exp(math.log(0.4) - 2.9957323 * jax.random.uniform(arg_keys[3], (GROUPS, GROUP_TOK, TOP), jnp.float32) ** steps_of(arg_keys[3], (GROUPS, GROUP_TOK, TOP), ((0, 32),), -0.2, 0.2)), 0.02, 0.4)
    gate_proj = gaussian(arg_keys[4], (EXPERTS, FF, D), D ** -0.5, 0.09375, ((0, 32), (1, 8)))
    up_proj = gaussian(arg_keys[5], (EXPERTS, FF, D), D ** -0.5, 0.09375, ((0, 32), (1, 8)))
    down_proj = gaussian(arg_keys[6], (EXPERTS, FF, D), FF ** -0.5, 0.15625, ((0, 32), (1, 8)))
    return {"tokens": tokens, "norm_gain": norm_gain, "expert_ids": expert_ids, "route_weights": route_weights, "gate_proj": gate_proj, "up_proj": up_proj, "down_proj": down_proj}


def rank_slots(id_table, expert_total):
    flat_ids = id_table.reshape(-1)
    onehot = (flat_ids[:, None] == jnp.arange(expert_total, dtype=jnp.int32)[None, :]).astype(jnp.int32)
    before = jnp.cumsum(onehot, axis=0) - onehot
    return lax.optimization_barrier(jnp.sum(before * onehot, axis=1)).reshape(id_table.shape).astype(jnp.int32)

def reference(tokens, norm_gain, expert_ids, route_weights, gate_proj, up_proj, down_proj):
    tok_float = tokens.astype(jnp.float32)
    inv_rms = lax.rsqrt(lax.optimization_barrier(jnp.mean(tok_float * tok_float, axis=-1, keepdims=True)) + 1e-06)
    normed = (tok_float * inv_rms * norm_gain.astype(jnp.float32)).astype(jnp.bfloat16)

    def group_ranks(id_table):
        return rank_slots(id_table, EXPERTS)
    slot_rank = jax.vmap(group_ranks)(expert_ids)
    slot_index = (expert_ids * MOST + slot_rank).astype(jnp.int32)
    token_order = jnp.broadcast_to(jnp.arange(GROUP_TOK, dtype=jnp.int32)[:, None], (GROUP_TOK, TOP))

    def build_tables(slot_row, weight_row):
        sources = jnp.full((EXPERTS * MOST,), GROUP_TOK, jnp.int32).at[slot_row.reshape(-1)].set(token_order.reshape(-1))
        slot_weights = jnp.zeros((EXPERTS * MOST,), jnp.float32).at[slot_row.reshape(-1)].set(weight_row.reshape(-1))
        return (sources, slot_weights)
    sources, slot_weights = jax.vmap(build_tables)(slot_index, route_weights)
    sources = sources.reshape(GROUPS, EXPERTS, MOST)
    slot_weights = slot_weights.reshape(GROUPS, EXPERTS, MOST)
    padded = jnp.concatenate([normed, jnp.zeros((GROUPS, 1, D), jnp.bfloat16)], axis=1)
    group_index = jnp.broadcast_to(jnp.arange(GROUPS, dtype=jnp.int32)[:, None], (GROUPS, MOST))
    block_count = FF // FF_DEV

    def one_expert(total, expert_no):
        pick_index = lax.dynamic_index_in_dim(sources, expert_no, axis=1, keepdims=False)
        pick_weights = lax.dynamic_index_in_dim(slot_weights, expert_no, axis=1, keepdims=False)
        rows = padded[group_index, pick_index].reshape(GROUPS * MOST, D).astype(jnp.float32)
        gate_act = jnp.einsum('rd,fd->rf', rows, gate_proj[expert_no].astype(jnp.float32), precision=lax.Precision.HIGHEST)
        up_act = jnp.einsum('rd,fd->rf', rows, up_proj[expert_no].astype(jnp.float32), precision=lax.Precision.HIGHEST)
        hidden = lax.optimization_barrier((jax.nn.silu(gate_act) * up_act).astype(jnp.bfloat16)).astype(jnp.float32)
        hidden_blocks = hidden.reshape(GROUPS * MOST, block_count, FF_DEV)
        down_blocks = down_proj[expert_no].astype(jnp.float32).reshape(block_count, FF_DEV, D)
        partial_value = jnp.einsum('rpf,pfd->rpd', hidden_blocks, down_blocks, precision=lax.Precision.HIGHEST)
        partial_value = lax.optimization_barrier(partial_value.astype(jnp.bfloat16)).astype(jnp.float32)
        summed = lax.optimization_barrier(jnp.sum(partial_value, axis=1)).reshape(GROUPS, MOST, D) * pick_weights[:, :, None]
        total = total.at[group_index, pick_index].add(summed, mode='drop')
        return (total, None)
    total_sum, ignored = lax.scan(one_expert, jnp.zeros((GROUPS, GROUP_TOK, D), jnp.float32), jnp.arange(EXPERTS, dtype=jnp.int32))
    return total_sum.astype(jnp.bfloat16)
```

```python
import jax
import jax.numpy as jnp
from jax import lax
from jax.sharding import PartitionSpec as P


def rank_slots(id_table, expert_total):
    flat_ids = id_table.reshape(-1)
    onehot = (flat_ids[:, None] == jnp.arange(expert_total, dtype=jnp.int32)[None, :]).astype(
        jnp.int32
    )
    before = jnp.cumsum(onehot, axis=0) - onehot
    return jnp.sum(before * onehot, axis=1).reshape(id_table.shape)


def body(tokens, norm_gain, expert_ids, route_weights, gate_proj, up_proj, down_proj):
    dp_count = lax.axis_size("dp")
    expert_count = lax.axis_size("expert")
    local_experts = gate_proj.shape[0]
    model_width = tokens.shape[2]
    group_ids = expert_ids[0]
    group_weights = route_weights[0]
    group_size = group_ids.shape[0]
    own_rows = group_size // dp_count
    top_k = group_ids.shape[1]
    experts = local_experts * expert_count
    capacity = dp_count * (group_size * top_k // (experts * dp_count) + 1)
    slot_count = experts * capacity
    tok_float = tokens[0].astype(jnp.float32)
    inv_rms = lax.rsqrt(jnp.mean(tok_float * tok_float, axis=-1, keepdims=True) + 1e-06)
    group_rows = (tok_float * inv_rms * norm_gain).astype(jnp.bfloat16)
    slot_rank = rank_slots(group_ids, experts)
    slot_index = group_ids * capacity + slot_rank
    hit = slot_index[None, :, :] == jnp.arange(slot_count, dtype=jnp.int32)[:, None, None]
    dispatch = jnp.any(hit, axis=2).astype(jnp.bfloat16)
    outgoing = jnp.dot(dispatch, group_rows, preferred_element_type=jnp.float32).astype(
        jnp.bfloat16
    )
    outgoing = outgoing.reshape(expert_count, local_experts, capacity, model_width)
    incoming = lax.all_to_all(outgoing, "expert", split_axis=0, concat_axis=0, tiled=True)
    gate_act = jnp.einsum("sjmd,jfd->sjmf", incoming, gate_proj, preferred_element_type=jnp.float32)
    up_act = jnp.einsum("sjmd,jfd->sjmf", incoming, up_proj, preferred_element_type=jnp.float32)
    hidden = (jax.nn.silu(gate_act) * up_act).astype(jnp.bfloat16)
    partial_rows = jnp.einsum(
        "sjmf,jfd->sjmd", hidden, down_proj, preferred_element_type=jnp.float32
    ).astype(jnp.bfloat16)
    returned = lax.all_to_all(partial_rows, "expert", split_axis=0, concat_axis=0, tiled=True)
    combine = jnp.sum(jnp.where(hit, group_weights[None, :, :], 0.0), axis=2)
    mixed_rows = jnp.dot(
        combine.T,
        returned.reshape(slot_count, model_width).astype(jnp.float32),
        precision=lax.Precision.HIGHEST,
        preferred_element_type=jnp.float32,
    )
    pieces = mixed_rows.astype(jnp.bfloat16).reshape(dp_count, own_rows, model_width)
    gathered = lax.all_to_all(pieces, "dp", split_axis=0, concat_axis=0, tiled=True)
    mixed = jnp.sum(gathered.astype(jnp.float32), axis=0).astype(jnp.bfloat16)
    return mixed[None]


def solution(mesh):
    placed = (
        P("expert", None, None),
        P(),
        P("expert", None, None),
        P("expert", None, None),
        P("expert", "dp", None),
        P("expert", "dp", None),
        P("expert", "dp", None),
    )
    return jax.shard_map(
        body, mesh=mesh, in_specs=placed, out_specs=P("expert", "dp", None), check_vma=False
    )
```

```python
import jax
import jax.numpy as jnp
from jax import lax
from jax.sharding import PartitionSpec as P


def rank_slots(id_table, expert_total):
    flat_ids = id_table.reshape(-1)
    onehot = (flat_ids[:, None] == jnp.arange(expert_total, dtype=jnp.int32)[None, :]).astype(
        jnp.int32
    )
    before = jnp.cumsum(onehot, axis=0) - onehot
    return jnp.sum(before * onehot, axis=1).reshape(id_table.shape)


def body(tokens, norm_gain, expert_ids, route_weights, gate_proj, up_proj, down_proj):
    dp_count = lax.axis_size("dp")
    expert_count = lax.axis_size("expert")
    local_experts = gate_proj.shape[0]
    model_width = tokens.shape[2]
    group_ids = expert_ids[0]
    group_weights = route_weights[0]
    group_size = group_ids.shape[0]
    own_rows = group_size // dp_count
    top_k = group_ids.shape[1]
    experts = local_experts * expert_count
    capacity = dp_count * (group_size * top_k // (experts * dp_count) + 1)
    slot_count = experts * capacity
    tok_float = tokens[0].astype(jnp.float32)
    inv_rms = lax.rsqrt(jnp.mean(tok_float * tok_float, axis=-1, keepdims=True) + 1e-06)
    group_rows = (tok_float * inv_rms * norm_gain).astype(jnp.bfloat16)
    slot_rank = rank_slots(group_ids, experts)
    slot_index = group_ids * capacity + slot_rank
    hit = slot_index[None, :, :] == jnp.arange(slot_count, dtype=jnp.int32)[:, None, None]
    dispatch = jnp.any(hit, axis=2).astype(jnp.bfloat16)
    outgoing = jnp.dot(dispatch, group_rows, preferred_element_type=jnp.float32).astype(
        jnp.bfloat16
    )
    outgoing = outgoing.reshape(expert_count, local_experts, capacity, model_width)
    incoming = lax.all_to_all(outgoing, "expert", split_axis=0, concat_axis=0, tiled=True)
    rows = incoming.reshape(slot_count, model_width)
    hidden_width = local_experts * gate_proj.shape[1]
    gate_act = jnp.dot(
        rows, gate_proj.reshape(hidden_width, model_width).T, preferred_element_type=jnp.float32
    )
    up_act = jnp.dot(
        rows, up_proj.reshape(hidden_width, model_width).T, preferred_element_type=jnp.float32
    )
    row_expert = (jnp.arange(rows.shape[0], dtype=jnp.int32) // capacity) % local_experts
    col_expert = jnp.arange(hidden_width, dtype=jnp.int32) // gate_proj.shape[1]
    own_block = row_expert[:, None] == col_expert[None, :]
    hidden = jnp.where(own_block, jax.nn.silu(gate_act) * up_act, 0.0).astype(jnp.bfloat16)
    partial_rows = jnp.dot(
        hidden, down_proj.reshape(hidden_width, model_width), preferred_element_type=jnp.float32
    ).astype(jnp.bfloat16)
    partial_rows = partial_rows.reshape(expert_count, local_experts, capacity, model_width)
    returned = lax.all_to_all(partial_rows, "expert", split_axis=0, concat_axis=0, tiled=True)
    combine = jnp.sum(jnp.where(hit, group_weights[None, :, :], 0.0), axis=2)
    combine_hi = combine.astype(jnp.bfloat16)
    combine_lo = (combine - combine_hi.astype(jnp.float32)).astype(jnp.bfloat16)
    flat_returned = returned.reshape(slot_count, model_width)
    mixed_rows = jnp.dot(
        combine_hi.T, flat_returned, preferred_element_type=jnp.float32
    ) + jnp.dot(combine_lo.T, flat_returned, preferred_element_type=jnp.float32)
    pieces = mixed_rows.astype(jnp.bfloat16).reshape(dp_count, own_rows, model_width)
    gathered = lax.all_to_all(pieces, "dp", split_axis=0, concat_axis=0, tiled=True)
    mixed = jnp.sum(gathered.astype(jnp.float32), axis=0).astype(jnp.bfloat16)
    return mixed[None]


def solution(mesh):
    placed = (
        P("expert", None, None),
        P(),
        P("expert", None, None),
        P("expert", None, None),
        P("expert", "dp", None),
        P("expert", "dp", None),
        P("expert", "dp", None),
    )
    return jax.shard_map(
        body, mesh=mesh, in_specs=placed, out_specs=P("expert", "dp", None), check_vma=False
    )
```

```python
import jax
import jax.numpy as jnp
from jax import lax
from jax.experimental import pallas as pl
from jax.sharding import PartitionSpec as P


def rank_slots(id_table, expert_total):
    flat_ids = id_table.reshape(-1)
    onehot = (flat_ids[:, None] == jnp.arange(expert_total, dtype=jnp.int32)[None, :]).astype(
        jnp.int32
    )
    before = jnp.cumsum(onehot, axis=0) - onehot
    return jnp.sum(before * onehot, axis=1).reshape(id_table.shape)


def ffn_block(x_ref, gate_ref, up_ref, down_ref, out_ref):
    width = x_ref.shape[3]
    rows = x_ref[...].reshape(x_ref.shape[0] * x_ref.shape[2], width)
    contract = (((1,), (1,)), ((), ()))
    gate_act = lax.dot_general(rows, gate_ref[0], contract, preferred_element_type=jnp.float32)
    up_act = lax.dot_general(rows, up_ref[0], contract, preferred_element_type=jnp.float32)
    hidden = (gate_act / (1.0 + jnp.exp(-gate_act)) * up_act).astype(jnp.bfloat16)
    partial = jnp.dot(hidden, down_ref[0], preferred_element_type=jnp.float32)
    out_ref[...] = partial.astype(out_ref.dtype).reshape(out_ref.shape)


def expert_ffn(incoming, gate_proj, up_proj, down_proj):
    sources, local_experts, capacity, width = incoming.shape
    hidden_width = gate_proj.shape[1]
    per_step = 8
    row_spec = pl.BlockSpec((per_step, 1, capacity, width), lambda j, b: (b, j, 0, 0))
    weight_spec = pl.BlockSpec((1, hidden_width, width), lambda j, b: (j, 0, 0))
    rows = sources * local_experts * capacity
    return pl.pallas_call(
        ffn_block,
        grid=(local_experts, sources // per_step),
        in_specs=[row_spec, weight_spec, weight_spec, weight_spec],
        out_specs=row_spec,
        out_shape=jax.ShapeDtypeStruct(incoming.shape, jnp.bfloat16),
        cost_estimate=pl.CostEstimate(
            flops=6 * rows * hidden_width * width,
            transcendentals=rows * hidden_width,
            bytes_accessed=4 * rows * width + 6 * local_experts * hidden_width * width,
        ),
    )(incoming, gate_proj, up_proj, down_proj)


def body(tokens, norm_gain, expert_ids, route_weights, gate_proj, up_proj, down_proj):
    dp_count = lax.axis_size("dp")
    expert_count = lax.axis_size("expert")
    local_experts = gate_proj.shape[0]
    model_width = tokens.shape[2]
    group_ids = expert_ids[0]
    group_weights = route_weights[0]
    group_size = group_ids.shape[0]
    own_rows = group_size // dp_count
    top_k = group_ids.shape[1]
    experts = local_experts * expert_count
    capacity = dp_count * (group_size * top_k // (experts * dp_count) + 1)
    slot_count = experts * capacity
    tok_float = tokens[0].astype(jnp.float32)
    inv_rms = lax.rsqrt(jnp.mean(tok_float * tok_float, axis=-1, keepdims=True) + 1e-06)
    group_rows = (tok_float * inv_rms * norm_gain).astype(jnp.bfloat16)
    slot_rank = rank_slots(group_ids, experts)
    slot_index = group_ids * capacity + slot_rank
    hit = slot_index[None, :, :] == jnp.arange(slot_count, dtype=jnp.int32)[:, None, None]
    dispatch = jnp.any(hit, axis=2).astype(jnp.bfloat16)
    outgoing = jnp.dot(dispatch, group_rows, preferred_element_type=jnp.float32).astype(
        jnp.bfloat16
    )
    outgoing = outgoing.reshape(expert_count, local_experts, capacity, model_width)
    incoming = lax.all_to_all(outgoing, "expert", split_axis=0, concat_axis=0, tiled=True)
    partial_rows = expert_ffn(incoming, gate_proj, up_proj, down_proj)
    returned = lax.all_to_all(partial_rows, "expert", split_axis=0, concat_axis=0, tiled=True)
    combine = jnp.sum(jnp.where(hit, group_weights[None, :, :], 0.0), axis=2)
    mixed_rows = jnp.dot(
        combine.T,
        returned.reshape(slot_count, model_width).astype(jnp.float32),
        precision=lax.Precision.HIGHEST,
        preferred_element_type=jnp.float32,
    )
    pieces = mixed_rows.astype(jnp.bfloat16).reshape(dp_count, own_rows, model_width)
    gathered = lax.all_to_all(pieces, "dp", split_axis=0, concat_axis=0, tiled=True)
    mixed = jnp.sum(gathered.astype(jnp.float32), axis=0).astype(jnp.bfloat16)
    return mixed[None]


def solution(mesh):
    placed = (
        P("expert", None, None),
        P(),
        P("expert", None, None),
        P("expert", None, None),
        P("expert", "dp", None),
        P("expert", "dp", None),
        P("expert", "dp", None),
    )
    return jax.shard_map(
        body, mesh=mesh, in_specs=placed, out_specs=P("expert", "dp", None), check_vma=False
    )
```

```python
import jax
import jax.numpy as jnp
from jax import lax
from jax.experimental import pallas as pl
from jax.sharding import PartitionSpec as P


def rank_slots(id_table, expert_total):
    flat_ids = id_table.reshape(-1)
    onehot = (flat_ids[:, None] == jnp.arange(expert_total, dtype=jnp.int32)[None, :]).astype(
        jnp.int32
    )
    before = jnp.cumsum(onehot, axis=0) - onehot
    return jnp.sum(before * onehot, axis=1).reshape(id_table.shape)


def ffn_block(x_ref, gate_ref, up_ref, down_ref, out_ref):
    width = x_ref.shape[3]
    rows = x_ref[...].reshape(x_ref.shape[0] * x_ref.shape[2], width)
    contract = (((1,), (1,)), ((), ()))
    gate_act = lax.dot_general(rows, gate_ref[0], contract, preferred_element_type=jnp.float32)
    up_act = lax.dot_general(rows, up_ref[0], contract, preferred_element_type=jnp.float32)
    hidden = (gate_act / (1.0 + jnp.exp(-gate_act)) * up_act).astype(jnp.bfloat16)
    partial = jnp.dot(hidden, down_ref[0], preferred_element_type=jnp.float32)
    out_ref[...] = partial.astype(out_ref.dtype).reshape(out_ref.shape)


def expert_ffn(incoming, gate_proj, up_proj, down_proj):
    sources, local_experts, capacity, width = incoming.shape
    hidden_width = gate_proj.shape[1]
    per_step = 8
    row_spec = pl.BlockSpec((per_step, 1, capacity, width), lambda j, b: (b, j, 0, 0))
    weight_spec = pl.BlockSpec((1, hidden_width, width), lambda j, b: (j, 0, 0))
    rows = sources * local_experts * capacity
    return pl.pallas_call(
        ffn_block,
        grid=(local_experts, sources // per_step),
        in_specs=[row_spec, weight_spec, weight_spec, weight_spec],
        out_specs=row_spec,
        out_shape=jax.ShapeDtypeStruct(incoming.shape, jnp.bfloat16),
        cost_estimate=pl.CostEstimate(
            flops=6 * rows * hidden_width * width,
            transcendentals=rows * hidden_width,
            bytes_accessed=4 * rows * width + 6 * local_experts * hidden_width * width,
        ),
    )(incoming, gate_proj, up_proj, down_proj)


def body(tokens, norm_gain, expert_ids, route_weights, gate_proj, up_proj, down_proj):
    dp_count = lax.axis_size("dp")
    expert_count = lax.axis_size("expert")
    local_experts = gate_proj.shape[0]
    model_width = tokens.shape[2]
    group_ids = expert_ids[0]
    group_weights = route_weights[0]
    group_size = group_ids.shape[0]
    own_rows = group_size // dp_count
    top_k = group_ids.shape[1]
    experts = local_experts * expert_count
    capacity = dp_count * (group_size * top_k // (experts * dp_count) + 1)
    slot_count = experts * capacity
    tok_float = tokens[0].astype(jnp.float32)
    inv_rms = lax.rsqrt(jnp.mean(tok_float * tok_float, axis=-1, keepdims=True) + 1e-06)
    group_rows = (tok_float * inv_rms * norm_gain).astype(jnp.bfloat16)
    slot_rank = rank_slots(group_ids, experts)
    slot_index = group_ids * capacity + slot_rank
    hit = slot_index[None, :, :] == jnp.arange(slot_count, dtype=jnp.int32)[:, None, None]
    dispatch = jnp.any(hit, axis=2).astype(jnp.bfloat16)
    outgoing = jnp.dot(dispatch, group_rows, preferred_element_type=jnp.float32).astype(
        jnp.bfloat16
    )
    outgoing = outgoing.reshape(expert_count, local_experts, capacity, model_width)
    combine = jnp.sum(jnp.where(hit, group_weights[None, :, :], 0.0), axis=2)
    combine, outgoing = lax.optimization_barrier((combine, outgoing))
    incoming = lax.all_to_all(outgoing, "expert", split_axis=0, concat_axis=0, tiled=True)
    partial_rows = expert_ffn(incoming, gate_proj, up_proj, down_proj)
    returned = lax.all_to_all(partial_rows, "expert", split_axis=0, concat_axis=0, tiled=True)
    mixed_rows = jnp.dot(
        combine.T,
        returned.reshape(slot_count, model_width).astype(jnp.float32),
        precision=lax.Precision.HIGHEST,
        preferred_element_type=jnp.float32,
    )
    pieces = mixed_rows.astype(jnp.bfloat16).reshape(dp_count, own_rows, model_width)
    gathered = lax.all_to_all(pieces, "dp", split_axis=0, concat_axis=0, tiled=True)
    mixed = jnp.sum(gathered.astype(jnp.float32), axis=0).astype(jnp.bfloat16)
    return mixed[None]


def solution(mesh):
    placed = (
        P("expert", None, None),
        P(),
        P("expert", None, None),
        P("expert", None, None),
        P("expert", "dp", None),
        P("expert", "dp", None),
        P("expert", "dp", None),
    )
    return jax.shard_map(
        body, mesh=mesh, in_specs=placed, out_specs=P("expert", "dp", None), check_vma=False
    )
```

```python
import jax
import jax.numpy as jnp
from jax import lax
from jax.experimental import pallas as pl
from jax.sharding import PartitionSpec as P


def rank_slots(id_table, expert_total):
    flat_ids = id_table.reshape(-1)
    onehot = (flat_ids[:, None] == jnp.arange(expert_total, dtype=jnp.int32)[None, :]).astype(
        jnp.int32
    )
    before = jnp.cumsum(onehot, axis=0) - onehot
    return jnp.sum(before * onehot, axis=1).reshape(id_table.shape)


def ffn_block(x_ref, gate_ref, up_ref, down_ref, out_ref):
    width = x_ref.shape[3]
    rows = x_ref[...].reshape(x_ref.shape[0] * x_ref.shape[2], width)
    contract = (((1,), (1,)), ((), ()))
    gate_act = lax.dot_general(rows, gate_ref[0], contract, preferred_element_type=jnp.float32)
    up_act = lax.dot_general(rows, up_ref[0], contract, preferred_element_type=jnp.float32)
    hidden = (gate_act / (1.0 + jnp.exp(-gate_act)) * up_act).astype(jnp.bfloat16)
    partial = jnp.dot(hidden, down_ref[0], preferred_element_type=jnp.float32)
    out_ref[...] = partial.astype(out_ref.dtype).reshape(out_ref.shape)


def expert_ffn(incoming, gate_proj, up_proj, down_proj):
    sources, local_experts, capacity, width = incoming.shape
    hidden_width = gate_proj.shape[1]
    per_step = 16
    row_spec = pl.BlockSpec((per_step, 1, capacity, width), lambda j, b: (b, j, 0, 0))
    weight_spec = pl.BlockSpec((1, hidden_width, width), lambda j, b: (j, 0, 0))
    rows = sources * local_experts * capacity
    return pl.pallas_call(
        ffn_block,
        grid=(local_experts, sources // per_step),
        in_specs=[row_spec, weight_spec, weight_spec, weight_spec],
        out_specs=row_spec,
        out_shape=jax.ShapeDtypeStruct(incoming.shape, jnp.bfloat16),
        cost_estimate=pl.CostEstimate(
            flops=6 * rows * hidden_width * width,
            transcendentals=rows * hidden_width,
            bytes_accessed=4 * rows * width + 6 * local_experts * hidden_width * width,
        ),
    )(incoming, gate_proj, up_proj, down_proj)


def body(tokens, norm_gain, expert_ids, route_weights, gate_proj, up_proj, down_proj):
    dp_count = lax.axis_size("dp")
    expert_count = lax.axis_size("expert")
    local_experts = gate_proj.shape[0]
    model_width = tokens.shape[2]
    group_ids = expert_ids[0]
    group_weights = route_weights[0]
    group_size = group_ids.shape[0]
    own_rows = group_size // dp_count
    top_k = group_ids.shape[1]
    experts = local_experts * expert_count
    capacity = dp_count * (group_size * top_k // (experts * dp_count) + 1)
    slot_count = experts * capacity
    tok_float = tokens[0].astype(jnp.float32)
    inv_rms = lax.rsqrt(jnp.mean(tok_float * tok_float, axis=-1, keepdims=True) + 1e-06)
    group_rows = (tok_float * inv_rms * norm_gain).astype(jnp.bfloat16)
    slot_rank = rank_slots(group_ids, experts)
    slot_index = group_ids * capacity + slot_rank
    hit = slot_index[None, :, :] == jnp.arange(slot_count, dtype=jnp.int32)[:, None, None]
    dispatch = jnp.any(hit, axis=2).astype(jnp.bfloat16)
    outgoing = jnp.dot(dispatch, group_rows, preferred_element_type=jnp.float32).astype(
        jnp.bfloat16
    )
    outgoing = outgoing.reshape(expert_count, local_experts, capacity, model_width)
    combine = jnp.sum(jnp.where(hit, group_weights[None, :, :], 0.0), axis=2)
    combine, outgoing = lax.optimization_barrier((combine, outgoing))
    incoming = lax.all_to_all(outgoing, "expert", split_axis=0, concat_axis=0, tiled=True)
    partial_rows = expert_ffn(incoming, gate_proj, up_proj, down_proj)
    returned = lax.all_to_all(partial_rows, "expert", split_axis=0, concat_axis=0, tiled=True)
    mixed_rows = jnp.dot(
        combine.T,
        returned.reshape(slot_count, model_width).astype(jnp.float32),
        precision=lax.Precision.HIGHEST,
        preferred_element_type=jnp.float32,
    )
    pieces = mixed_rows.astype(jnp.bfloat16).reshape(dp_count, own_rows, model_width)
    gathered = lax.all_to_all(pieces, "dp", split_axis=0, concat_axis=0, tiled=True)
    mixed = jnp.sum(gathered.astype(jnp.float32), axis=0).astype(jnp.bfloat16)
    return mixed[None]


def solution(mesh):
    placed = (
        P("expert", None, None),
        P(),
        P("expert", None, None),
        P("expert", None, None),
        P("expert", "dp", None),
        P("expert", "dp", None),
        P("expert", "dp", None),
    )
    return jax.shard_map(
        body, mesh=mesh, in_specs=placed, out_specs=P("expert", "dp", None), check_vma=False
    )
```

```python
import jax
import jax.numpy as jnp
from jax import lax
from jax.experimental import pallas as pl
from jax.sharding import PartitionSpec as P


def rank_slots(id_table, expert_total):
    flat_ids = id_table.reshape(-1)
    onehot = (flat_ids[:, None] == jnp.arange(expert_total, dtype=jnp.int32)[None, :]).astype(
        jnp.int32
    )
    before = jnp.cumsum(onehot, axis=0) - onehot
    return jnp.sum(before * onehot, axis=1).reshape(id_table.shape)


def ffn_block(x_ref, gate_ref, up_ref, down_ref, out_ref):
    width = x_ref.shape[3]
    rows = x_ref[...].reshape(x_ref.shape[0] * x_ref.shape[2], width)
    contract = (((1,), (1,)), ((), ()))
    gate_act = lax.dot_general(rows, gate_ref[0], contract, preferred_element_type=jnp.float32)
    up_act = lax.dot_general(rows, up_ref[0], contract, preferred_element_type=jnp.float32)
    hidden = (gate_act / (1.0 + jnp.exp(-gate_act)) * up_act).astype(jnp.bfloat16)
    partial = jnp.dot(hidden, down_ref[0], preferred_element_type=jnp.float32)
    out_ref[...] = partial.astype(out_ref.dtype).reshape(out_ref.shape)


def expert_ffn(incoming, gate_proj, up_proj, down_proj):
    sources, local_experts, capacity, width = incoming.shape
    hidden_width = gate_proj.shape[1]
    per_step = 16
    row_spec = pl.BlockSpec((per_step, 1, capacity, width), lambda j, b: (b, j, 0, 0))
    weight_spec = pl.BlockSpec((1, hidden_width, width), lambda j, b: (j, 0, 0))
    rows = sources * local_experts * capacity
    return pl.pallas_call(
        ffn_block,
        grid=(local_experts, sources // per_step),
        in_specs=[row_spec, weight_spec, weight_spec, weight_spec],
        out_specs=row_spec,
        out_shape=jax.ShapeDtypeStruct(incoming.shape, jnp.bfloat16),
        cost_estimate=pl.CostEstimate(
            flops=6 * rows * hidden_width * width,
            transcendentals=rows * hidden_width,
            bytes_accessed=4 * rows * width + 6 * local_experts * hidden_width * width,
        ),
    )(incoming, gate_proj, up_proj, down_proj)


def body(tokens, norm_gain, expert_ids, route_weights, gate_proj, up_proj, down_proj):
    dp_count = lax.axis_size("dp")
    expert_count = lax.axis_size("expert")
    local_experts = gate_proj.shape[0]
    model_width = tokens.shape[2]
    group_ids = expert_ids[0]
    group_weights = route_weights[0]
    group_size = group_ids.shape[0]
    own_rows = group_size // dp_count
    top_k = group_ids.shape[1]
    experts = local_experts * expert_count
    capacity = dp_count * (group_size * top_k // (experts * dp_count) + 1)
    slot_count = experts * capacity
    tok_float = tokens[0].astype(jnp.float32)
    inv_rms = lax.rsqrt(jnp.mean(tok_float * tok_float, axis=-1, keepdims=True) + 1e-06)
    group_rows = (tok_float * inv_rms * norm_gain).astype(jnp.bfloat16)
    slot_rank = rank_slots(group_ids, experts)
    slot_index = group_ids * capacity + slot_rank
    hit = slot_index[None, :, :] == jnp.arange(slot_count, dtype=jnp.int32)[:, None, None]
    dispatch = jnp.any(hit, axis=2).astype(jnp.bfloat16)
    outgoing = jnp.dot(dispatch, group_rows, preferred_element_type=jnp.float32).astype(
        jnp.bfloat16
    )
    outgoing = outgoing.reshape(expert_count, local_experts, capacity, model_width)
    combine = jnp.sum(jnp.where(hit, group_weights[None, :, :], 0.0), axis=2)
    place = lax.axis_index("dp")
    combine = jnp.roll(combine, -own_rows * place, axis=1)
    combine, outgoing = lax.optimization_barrier((combine, outgoing))
    incoming = lax.all_to_all(outgoing, "expert", split_axis=0, concat_axis=0, tiled=True)
    partial_rows = expert_ffn(incoming, gate_proj, up_proj, down_proj)
    returned = lax.all_to_all(partial_rows, "expert", split_axis=0, concat_axis=0, tiled=True)
    mixed_rows = jnp.dot(
        combine.T,
        returned.reshape(slot_count, model_width).astype(jnp.float32),
        precision=lax.Precision.HIGHEST,
        preferred_element_type=jnp.float32,
    )
    pieces = mixed_rows.astype(jnp.bfloat16).reshape(dp_count, own_rows, model_width)
    total = pieces[0].astype(jnp.float32)
    for shift in range(1, dp_count):
        inbound = lax.ppermute(
            pieces[shift], "dp", [(i, (i + shift) % dp_count) for i in range(dp_count)]
        )
        total = total + inbound.astype(jnp.float32)
    mixed = total.astype(jnp.bfloat16)
    return mixed[None]


def solution(mesh):
    placed = (
        P("expert", None, None),
        P(),
        P("expert", None, None),
        P("expert", None, None),
        P("expert", "dp", None),
        P("expert", "dp", None),
        P("expert", "dp", None),
    )
    return jax.shard_map(
        body, mesh=mesh, in_specs=placed, out_specs=P("expert", "dp", None), check_vma=False
    )
```

```python
import jax
import jax.numpy as jnp
from jax import lax
from jax.experimental import pallas as pl
from jax.sharding import PartitionSpec as P


def rank_slots(id_table, expert_total):
    flat_ids = id_table.reshape(-1)
    onehot = (flat_ids[:, None] == jnp.arange(expert_total, dtype=jnp.int32)[None, :]).astype(
        jnp.int32
    )
    before = jnp.cumsum(onehot, axis=0) - onehot
    return jnp.sum(before * onehot, axis=1).reshape(id_table.shape)


def ffn_block(x_ref, gate_ref, up_ref, down_ref, out_ref):
    width = x_ref.shape[3]
    rows = x_ref[...].reshape(x_ref.shape[0] * x_ref.shape[2], width)
    contract = (((1,), (1,)), ((), ()))
    gate_act = lax.dot_general(rows, gate_ref[0], contract, preferred_element_type=jnp.float32)
    up_act = lax.dot_general(rows, up_ref[0], contract, preferred_element_type=jnp.float32)
    hidden = (gate_act / (1.0 + jnp.exp(-gate_act)) * up_act).astype(jnp.bfloat16)
    partial = jnp.dot(hidden, down_ref[0], preferred_element_type=jnp.float32)
    out_ref[...] = partial.astype(out_ref.dtype).reshape(out_ref.shape)


def expert_ffn(incoming, gate_proj, up_proj, down_proj):
    sources, local_experts, capacity, width = incoming.shape
    hidden_width = gate_proj.shape[1]
    per_step = 32
    row_spec = pl.BlockSpec((per_step, 1, capacity, width), lambda j, b: (b, j, 0, 0))
    weight_spec = pl.BlockSpec((1, hidden_width, width), lambda j, b: (j, 0, 0))
    rows = sources * local_experts * capacity
    return pl.pallas_call(
        ffn_block,
        grid=(local_experts, sources // per_step),
        in_specs=[row_spec, weight_spec, weight_spec, weight_spec],
        out_specs=row_spec,
        out_shape=jax.ShapeDtypeStruct(incoming.shape, jnp.bfloat16),
        cost_estimate=pl.CostEstimate(
            flops=6 * rows * hidden_width * width,
            transcendentals=rows * hidden_width,
            bytes_accessed=4 * rows * width + 6 * local_experts * hidden_width * width,
        ),
    )(incoming, gate_proj, up_proj, down_proj)


def body(tokens, norm_gain, expert_ids, route_weights, gate_proj, up_proj, down_proj):
    dp_count = lax.axis_size("dp")
    expert_count = lax.axis_size("expert")
    local_experts = gate_proj.shape[0]
    model_width = tokens.shape[2]
    group_ids = expert_ids[0]
    group_weights = route_weights[0]
    group_size = group_ids.shape[0]
    own_rows = group_size // dp_count
    top_k = group_ids.shape[1]
    experts = local_experts * expert_count
    capacity = dp_count * (group_size * top_k // (experts * dp_count) + 1)
    slot_count = experts * capacity
    tok_float = tokens[0].astype(jnp.float32)
    inv_rms = lax.rsqrt(jnp.mean(tok_float * tok_float, axis=-1, keepdims=True) + 1e-06)
    group_rows = (tok_float * inv_rms * norm_gain).astype(jnp.bfloat16)
    slot_rank = rank_slots(group_ids, experts)
    slot_index = group_ids * capacity + slot_rank
    hit = slot_index[None, :, :] == jnp.arange(slot_count, dtype=jnp.int32)[:, None, None]
    dispatch = jnp.any(hit, axis=2).astype(jnp.bfloat16)
    outgoing = jnp.dot(dispatch, group_rows, preferred_element_type=jnp.float32).astype(
        jnp.bfloat16
    )
    outgoing = outgoing.reshape(expert_count, local_experts, capacity, model_width)
    combine = jnp.sum(jnp.where(hit, group_weights[None, :, :], 0.0), axis=2)
    combine, outgoing = lax.optimization_barrier((combine, outgoing))
    incoming = lax.all_to_all(outgoing, "expert", split_axis=0, concat_axis=0, tiled=True)
    partial_rows = expert_ffn(incoming, gate_proj, up_proj, down_proj)
    returned = lax.all_to_all(partial_rows, "expert", split_axis=0, concat_axis=0, tiled=True)
    mixed_rows = jnp.dot(
        combine.T,
        returned.reshape(slot_count, model_width).astype(jnp.float32),
        precision=lax.Precision.HIGHEST,
        preferred_element_type=jnp.float32,
    )
    pieces = mixed_rows.astype(jnp.bfloat16).reshape(dp_count, own_rows, model_width)
    gathered = lax.all_to_all(pieces, "dp", split_axis=0, concat_axis=0, tiled=True)
    mixed = jnp.sum(gathered.astype(jnp.float32), axis=0).astype(jnp.bfloat16)
    return mixed[None]


def solution(mesh):
    placed = (
        P("expert", None, None),
        P(),
        P("expert", None, None),
        P("expert", None, None),
        P("expert", "dp", None),
        P("expert", "dp", None),
        P("expert", "dp", None),
    )
    return jax.shard_map(
        body, mesh=mesh, in_specs=placed, out_specs=P("expert", "dp", None), check_vma=False
    )
```

```python
import jax
import jax.numpy as jnp
from jax import lax
from jax.experimental import pallas as pl
from jax.sharding import PartitionSpec as P


def rank_slots(id_table, expert_total):
    flat_ids = id_table.reshape(-1)
    onehot = (flat_ids[:, None] == jnp.arange(expert_total, dtype=jnp.int32)[None, :]).astype(
        jnp.int32
    )
    before = jnp.cumsum(onehot, axis=0) - onehot
    return jnp.sum(before * onehot, axis=1).reshape(id_table.shape)


def ffn_block(x_ref, gate_ref, up_ref, down_ref, out_ref):
    width = x_ref.shape[3]
    rows = x_ref[...].reshape(x_ref.shape[0] * x_ref.shape[2], width)
    contract = (((1,), (1,)), ((), ()))
    gate_act = lax.dot_general(rows, gate_ref[0], contract, preferred_element_type=jnp.float32)
    up_act = lax.dot_general(rows, up_ref[0], contract, preferred_element_type=jnp.float32)
    hidden = (gate_act / (1.0 + jnp.exp(-gate_act)) * up_act).astype(jnp.bfloat16)
    partial = jnp.dot(hidden, down_ref[0], preferred_element_type=jnp.float32)
    out_ref[...] = partial.astype(out_ref.dtype).reshape(out_ref.shape)


def expert_ffn(incoming, gate_proj, up_proj, down_proj):
    sources, local_experts, capacity, width = incoming.shape
    hidden_width = gate_proj.shape[1]
    per_step = 32
    row_spec = pl.BlockSpec((per_step, 1, capacity, width), lambda j, b: (b, j, 0, 0))
    weight_spec = pl.BlockSpec((1, hidden_width, width), lambda j, b: (j, 0, 0))
    rows = sources * local_experts * capacity
    return pl.pallas_call(
        ffn_block,
        grid=(local_experts, sources // per_step),
        in_specs=[row_spec, weight_spec, weight_spec, weight_spec],
        out_specs=row_spec,
        out_shape=jax.ShapeDtypeStruct(incoming.shape, jnp.bfloat16),
        cost_estimate=pl.CostEstimate(
            flops=6 * rows * hidden_width * width,
            transcendentals=rows * hidden_width,
            bytes_accessed=4 * rows * width + 6 * local_experts * hidden_width * width,
        ),
    )(incoming, gate_proj, up_proj, down_proj)


def body(tokens, norm_gain, expert_ids, route_weights, gate_proj, up_proj, down_proj):
    dp_count = lax.axis_size("dp")
    expert_count = lax.axis_size("expert")
    local_experts = gate_proj.shape[0]
    model_width = tokens.shape[2]
    group_ids = expert_ids[0]
    group_weights = route_weights[0]
    group_size = group_ids.shape[0]
    own_rows = group_size // dp_count
    top_k = group_ids.shape[1]
    experts = local_experts * expert_count
    capacity = dp_count * (group_size * top_k // (experts * dp_count) + 1)
    slot_count = experts * capacity
    tok_float = tokens[0].astype(jnp.float32)
    inv_rms = lax.rsqrt(jnp.mean(tok_float * tok_float, axis=-1, keepdims=True) + 1e-06)
    group_rows = (tok_float * inv_rms * norm_gain).astype(jnp.bfloat16)
    slot_rank = rank_slots(group_ids, experts)
    slot_index = group_ids * capacity + slot_rank
    hit = slot_index[None, :, :] == jnp.arange(slot_count, dtype=jnp.int32)[:, None, None]
    dispatch = jnp.any(hit, axis=2).astype(jnp.bfloat16)
    outgoing = jnp.dot(dispatch, group_rows, preferred_element_type=jnp.float32).astype(
        jnp.bfloat16
    )
    outgoing = outgoing.reshape(expert_count, local_experts, capacity, model_width)
    combine = jnp.sum(jnp.where(hit, group_weights[None, :, :], 0.0), axis=2)
    combine_hi = combine.astype(jnp.bfloat16)
    combine_lo = (combine - combine_hi.astype(jnp.float32)).astype(jnp.bfloat16)
    stacked = jnp.concatenate([combine_hi, combine_lo], axis=1)
    stacked, outgoing = lax.optimization_barrier((stacked, outgoing))
    incoming = lax.all_to_all(outgoing, "expert", split_axis=0, concat_axis=0, tiled=True)
    partial_rows = expert_ffn(incoming, gate_proj, up_proj, down_proj)
    returned = lax.all_to_all(partial_rows, "expert", split_axis=0, concat_axis=0, tiled=True)
    both_parts = jnp.dot(
        stacked.T, returned.reshape(slot_count, model_width), preferred_element_type=jnp.float32
    )
    mixed_rows = both_parts[:group_size] + both_parts[group_size:]
    pieces = mixed_rows.astype(jnp.bfloat16).reshape(dp_count, own_rows, model_width)
    gathered = lax.all_to_all(pieces, "dp", split_axis=0, concat_axis=0, tiled=True)
    mixed = jnp.sum(gathered.astype(jnp.float32), axis=0).astype(jnp.bfloat16)
    return mixed[None]


def solution(mesh):
    placed = (
        P("expert", None, None),
        P(),
        P("expert", None, None),
        P("expert", None, None),
        P("expert", "dp", None),
        P("expert", "dp", None),
        P("expert", "dp", None),
    )
    return jax.shard_map(
        body, mesh=mesh, in_specs=placed, out_specs=P("expert", "dp", None), check_vma=False
    )
```

```python
import jax
import jax.numpy as jnp
from jax import lax
from jax.experimental import pallas as pl
from jax.sharding import PartitionSpec as P


def ffn_block(x_ref, gate_ref, up_ref, down_ref, out_ref):
    width = x_ref.shape[3]
    rows = x_ref[...].reshape(x_ref.shape[0] * x_ref.shape[2], width)
    contract = (((1,), (1,)), ((), ()))
    gate_act = lax.dot_general(rows, gate_ref[0], contract, preferred_element_type=jnp.float32)
    up_act = lax.dot_general(rows, up_ref[0], contract, preferred_element_type=jnp.float32)
    hidden = (gate_act / (1.0 + jnp.exp(-gate_act)) * up_act).astype(jnp.bfloat16)
    partial = jnp.dot(hidden, down_ref[0], preferred_element_type=jnp.float32)
    out_ref[...] = partial.astype(out_ref.dtype).reshape(out_ref.shape)


def expert_ffn(incoming, gate_proj, up_proj, down_proj):
    sources, local_experts, capacity, width = incoming.shape
    hidden_width = gate_proj.shape[1]
    per_step = 32
    row_spec = pl.BlockSpec((per_step, 1, capacity, width), lambda j, b: (b, j, 0, 0))
    weight_spec = pl.BlockSpec((1, hidden_width, width), lambda j, b: (j, 0, 0))
    rows = sources * local_experts * capacity
    return pl.pallas_call(
        ffn_block,
        grid=(local_experts, sources // per_step),
        in_specs=[row_spec, weight_spec, weight_spec, weight_spec],
        out_specs=row_spec,
        out_shape=jax.ShapeDtypeStruct(incoming.shape, jnp.bfloat16),
        cost_estimate=pl.CostEstimate(
            flops=6 * rows * hidden_width * width,
            transcendentals=rows * hidden_width,
            bytes_accessed=4 * rows * width + 6 * local_experts * hidden_width * width,
        ),
    )(incoming, gate_proj, up_proj, down_proj)


def body(tokens, norm_gain, expert_ids, route_weights, gate_proj, up_proj, down_proj):
    dp_count = lax.axis_size("dp")
    expert_count = lax.axis_size("expert")
    local_experts = gate_proj.shape[0]
    model_width = tokens.shape[2]
    group_ids = expert_ids[0]
    group_weights = route_weights[0]
    group_size = group_ids.shape[0]
    own_rows = group_size // dp_count
    top_k = group_ids.shape[1]
    experts = local_experts * expert_count
    capacity = dp_count * (group_size * top_k // (experts * dp_count) + 1)
    slot_count = experts * capacity
    tok_float = tokens[0].astype(jnp.float32)
    inv_rms = lax.rsqrt(jnp.mean(tok_float * tok_float, axis=-1, keepdims=True) + 1e-06)
    group_rows = (tok_float * inv_rms * norm_gain).astype(jnp.bfloat16)
    chosen = group_ids[:, :, None] == jnp.arange(experts, dtype=jnp.int32)[None, None, :]
    picks = jnp.any(chosen, axis=1)
    weight_of = jnp.sum(jnp.where(chosen, group_weights[:, :, None], 0.0), axis=1)
    token_at = jnp.arange(group_size, dtype=jnp.int32)
    earlier = (token_at[:, None] > token_at[None, :]).astype(jnp.bfloat16)
    rank = jnp.dot(earlier, picks.astype(jnp.bfloat16), preferred_element_type=jnp.float32)
    place_hit = picks[:, :, None] & (
        rank.astype(jnp.int32)[:, :, None] == jnp.arange(capacity, dtype=jnp.int32)[None, None, :]
    )
    slot_hit = jnp.transpose(place_hit, (1, 2, 0)).reshape(slot_count, group_size)
    dispatch = slot_hit.astype(jnp.bfloat16)
    combine = jnp.where(
        slot_hit, jnp.repeat(weight_of.T, capacity, axis=0), 0.0
    )
    outgoing = jnp.dot(dispatch, group_rows, preferred_element_type=jnp.float32).astype(
        jnp.bfloat16
    )
    outgoing = outgoing.reshape(expert_count, local_experts, capacity, model_width)
    combine_hi = combine.astype(jnp.bfloat16)
    combine_lo = (combine - combine_hi.astype(jnp.float32)).astype(jnp.bfloat16)
    stacked = jnp.concatenate([combine_hi, combine_lo], axis=1)
    stacked, outgoing = lax.optimization_barrier((stacked, outgoing))
    incoming = lax.all_to_all(outgoing, "expert", split_axis=0, concat_axis=0, tiled=True)
    partial_rows = expert_ffn(incoming, gate_proj, up_proj, down_proj)
    returned = lax.all_to_all(partial_rows, "expert", split_axis=0, concat_axis=0, tiled=True)
    both_parts = jnp.dot(
        stacked.T, returned.reshape(slot_count, model_width), preferred_element_type=jnp.float32
    )
    mixed_rows = both_parts[:group_size] + both_parts[group_size:]
    pieces = mixed_rows.astype(jnp.bfloat16).reshape(dp_count, own_rows, model_width)
    gathered = lax.all_to_all(pieces, "dp", split_axis=0, concat_axis=0, tiled=True)
    mixed = jnp.sum(gathered.astype(jnp.float32), axis=0).astype(jnp.bfloat16)
    return mixed[None]


def solution(mesh):
    placed = (
        P("expert", None, None),
        P(),
        P("expert", None, None),
        P("expert", None, None),
        P("expert", "dp", None),
        P("expert", "dp", None),
        P("expert", "dp", None),
    )
    return jax.shard_map(
        body, mesh=mesh, in_specs=placed, out_specs=P("expert", "dp", None), check_vma=False
    )
```

```python
import jax
import jax.numpy as jnp
from jax import lax
from jax.experimental import pallas as pl
from jax.sharding import PartitionSpec as P


def ffn_block(x_ref, gate_ref, up_ref, down_ref, out_ref):
    width = x_ref.shape[3]
    rows = x_ref[...].reshape(x_ref.shape[0] * x_ref.shape[2], width)
    contract = (((1,), (1,)), ((), ()))
    gate_act = lax.dot_general(rows, gate_ref[0], contract, preferred_element_type=jnp.float32)
    up_act = lax.dot_general(rows, up_ref[0], contract, preferred_element_type=jnp.float32)
    hidden = (gate_act / (1.0 + jnp.exp(-gate_act)) * up_act).astype(jnp.bfloat16)
    partial = jnp.dot(hidden, down_ref[0], preferred_element_type=jnp.float32)
    out_ref[...] = partial.astype(out_ref.dtype).reshape(out_ref.shape)


def expert_ffn(incoming, gate_proj, up_proj, down_proj):
    sources, local_experts, capacity, width = incoming.shape
    hidden_width = gate_proj.shape[1]
    per_step = 32
    row_spec = pl.BlockSpec((per_step, 1, capacity, width), lambda j, b: (b, j, 0, 0))
    weight_spec = pl.BlockSpec((1, hidden_width, width), lambda j, b: (j, 0, 0))
    rows = sources * local_experts * capacity
    return pl.pallas_call(
        ffn_block,
        grid=(local_experts, sources // per_step),
        in_specs=[row_spec, weight_spec, weight_spec, weight_spec],
        out_specs=row_spec,
        out_shape=jax.ShapeDtypeStruct(incoming.shape, jnp.bfloat16),
        cost_estimate=pl.CostEstimate(
            flops=6 * rows * hidden_width * width,
            transcendentals=rows * hidden_width,
            bytes_accessed=4 * rows * width + 6 * local_experts * hidden_width * width,
        ),
    )(incoming, gate_proj, up_proj, down_proj)


def body(tokens, norm_gain, expert_ids, route_weights, gate_proj, up_proj, down_proj):
    dp_count = lax.axis_size("dp")
    expert_count = lax.axis_size("expert")
    local_experts = gate_proj.shape[0]
    model_width = tokens.shape[2]
    group_ids = expert_ids[0]
    group_weights = route_weights[0]
    group_size = group_ids.shape[0]
    own_rows = group_size // dp_count
    top_k = group_ids.shape[1]
    experts = local_experts * expert_count
    capacity = dp_count * (group_size * top_k // (experts * dp_count) + 1)
    slot_count = experts * capacity
    tok_float = tokens[0].astype(jnp.float32)
    inv_rms = lax.rsqrt(jnp.mean(tok_float * tok_float, axis=-1, keepdims=True) + 1e-06)
    group_rows = (tok_float * inv_rms * norm_gain).astype(jnp.bfloat16)
    expert_at = jnp.arange(experts, dtype=jnp.int32)[None, :]
    picks = jnp.zeros((group_size, experts), jnp.bool_)
    weight_of = jnp.zeros((group_size, experts), jnp.float32)
    for choice in range(top_k):
        named = group_ids[:, choice : choice + 1] == expert_at
        picks = picks | named
        weight_of = weight_of + jnp.where(named, group_weights[:, choice : choice + 1], 0.0)
    token_at = jnp.arange(group_size, dtype=jnp.int32)
    earlier = (token_at[:, None] > token_at[None, :]).astype(jnp.bfloat16)
    rank = jnp.dot(earlier, picks.astype(jnp.bfloat16), preferred_element_type=jnp.float32)
    place_hit = picks[:, :, None] & (
        rank.astype(jnp.int32)[:, :, None] == jnp.arange(capacity, dtype=jnp.int32)[None, None, :]
    )
    slot_hit = jnp.transpose(place_hit, (1, 2, 0)).reshape(slot_count, group_size)
    dispatch = slot_hit.astype(jnp.bfloat16)
    combine = jnp.where(
        slot_hit, jnp.repeat(weight_of.T, capacity, axis=0), 0.0
    )
    outgoing = jnp.dot(dispatch, group_rows, preferred_element_type=jnp.float32).astype(
        jnp.bfloat16
    )
    outgoing = outgoing.reshape(expert_count, local_experts, capacity, model_width)
    combine_hi = combine.astype(jnp.bfloat16)
    combine_lo = (combine - combine_hi.astype(jnp.float32)).astype(jnp.bfloat16)
    stacked = jnp.concatenate([combine_hi, combine_lo], axis=1)
    stacked, outgoing = lax.optimization_barrier((stacked, outgoing))
    incoming = lax.all_to_all(outgoing, "expert", split_axis=0, concat_axis=0, tiled=True)
    partial_rows = expert_ffn(incoming, gate_proj, up_proj, down_proj)
    returned = lax.all_to_all(partial_rows, "expert", split_axis=0, concat_axis=0, tiled=True)
    both_parts = jnp.dot(
        stacked.T, returned.reshape(slot_count, model_width), preferred_element_type=jnp.float32
    )
    mixed_rows = both_parts[:group_size] + both_parts[group_size:]
    pieces = mixed_rows.astype(jnp.bfloat16).reshape(dp_count, own_rows, model_width)
    gathered = lax.all_to_all(pieces, "dp", split_axis=0, concat_axis=0, tiled=True)
    mixed = jnp.sum(gathered.astype(jnp.float32), axis=0).astype(jnp.bfloat16)
    return mixed[None]


def solution(mesh):
    placed = (
        P("expert", None, None),
        P(),
        P("expert", None, None),
        P("expert", None, None),
        P("expert", "dp", None),
        P("expert", "dp", None),
        P("expert", "dp", None),
    )
    return jax.shard_map(
        body, mesh=mesh, in_specs=placed, out_specs=P("expert", "dp", None), check_vma=False
    )
```

```python
import jax
import jax.numpy as jnp
from jax import lax
from jax.experimental import pallas as pl
from jax.experimental.pallas import tpu as pltpu
from jax.sharding import PartitionSpec as P


def ffn_block(x_ref, gate_ref, up_ref, down_ref, out_ref, hidden_ref):
    @pl.when(pl.program_id(1) == 0)
    def _():
        width = x_ref.shape[3]
        rows = x_ref[...].reshape(x_ref.shape[0] * x_ref.shape[2], width)
        contract = (((1,), (1,)), ((), ()))
        gate_act = lax.dot_general(rows, gate_ref[0], contract, preferred_element_type=jnp.float32)
        up_act = lax.dot_general(rows, up_ref[0], contract, preferred_element_type=jnp.float32)
        hidden_ref[...] = (gate_act / (1.0 + jnp.exp(-gate_act)) * up_act).astype(jnp.bfloat16)

    partial = jnp.dot(hidden_ref[...], down_ref[0], preferred_element_type=jnp.float32)
    out_ref[...] = partial.astype(out_ref.dtype).reshape(out_ref.shape)


def expert_ffn(incoming, gate_proj, up_proj, down_proj):
    sources, local_experts, capacity, width = incoming.shape
    hidden_width = gate_proj.shape[1]
    halves = 2
    rows = sources * local_experts * capacity
    x_spec = pl.BlockSpec((sources, 1, capacity, width), lambda j, c: (0, j, 0, 0))
    weight_spec = pl.BlockSpec((1, hidden_width, width), lambda j, c: (j, 0, 0))
    down_spec = pl.BlockSpec((1, hidden_width, width // halves), lambda j, c: (j, 0, c))
    out_spec = pl.BlockSpec((sources, 1, capacity, width // halves), lambda j, c: (0, j, 0, c))
    return pl.pallas_call(
        ffn_block,
        grid=(local_experts, halves),
        in_specs=[x_spec, weight_spec, weight_spec, down_spec],
        out_specs=out_spec,
        out_shape=jax.ShapeDtypeStruct(incoming.shape, jnp.bfloat16),
        scratch_shapes=[pltpu.VMEM((sources * capacity, hidden_width), jnp.bfloat16)],
        cost_estimate=pl.CostEstimate(
            flops=6 * rows * hidden_width * width,
            transcendentals=rows * hidden_width,
            bytes_accessed=4 * rows * width + 6 * local_experts * hidden_width * width,
        ),
    )(incoming, gate_proj, up_proj, down_proj)


def body(tokens, norm_gain, expert_ids, route_weights, gate_proj, up_proj, down_proj):
    dp_count = lax.axis_size("dp")
    expert_count = lax.axis_size("expert")
    local_experts = gate_proj.shape[0]
    model_width = tokens.shape[2]
    group_ids = expert_ids[0]
    group_weights = route_weights[0]
    group_size = group_ids.shape[0]
    own_rows = group_size // dp_count
    top_k = group_ids.shape[1]
    experts = local_experts * expert_count
    capacity = dp_count * (group_size * top_k // (experts * dp_count) + 1)
    slot_count = experts * capacity
    tok_float = tokens[0].astype(jnp.float32)
    gram = lax.dot_general(
        tokens[0], tokens[0], (((1,), (1,)), ((), ())), preferred_element_type=jnp.float32
    )
    squares = jnp.sum(jnp.where(jnp.eye(gram.shape[0], dtype=jnp.bool_), gram, 0.0), axis=1)
    inv_rms = lax.rsqrt(squares[:, None] / model_width + 1e-06)
    group_rows = (tok_float * inv_rms * norm_gain).astype(jnp.bfloat16)
    expert_at = jnp.arange(experts, dtype=jnp.int32)[None, :]
    picks = jnp.zeros((group_size, experts), jnp.bool_)
    weight_of = jnp.zeros((group_size, experts), jnp.float32)
    for choice in range(top_k):
        named = group_ids[:, choice : choice + 1] == expert_at
        picks = picks | named
        weight_of = weight_of + jnp.where(named, group_weights[:, choice : choice + 1], 0.0)
    token_at = jnp.arange(group_size, dtype=jnp.int32)
    earlier = (token_at[:, None] > token_at[None, :]).astype(jnp.bfloat16)
    rank = jnp.dot(earlier, picks.astype(jnp.bfloat16), preferred_element_type=jnp.float32)
    place_hit = picks[:, :, None] & (
        rank.astype(jnp.int32)[:, :, None] == jnp.arange(capacity, dtype=jnp.int32)[None, None, :]
    )
    slot_hit = jnp.transpose(place_hit, (1, 2, 0)).reshape(slot_count, group_size)
    dispatch = slot_hit.astype(jnp.bfloat16)
    combine = jnp.where(
        slot_hit, jnp.repeat(weight_of.T, capacity, axis=0), 0.0
    )
    outgoing = jnp.dot(dispatch, group_rows, preferred_element_type=jnp.float32).astype(
        jnp.bfloat16
    )
    outgoing = outgoing.reshape(expert_count, local_experts, capacity, model_width)
    combine_hi = combine.astype(jnp.bfloat16)
    combine_lo = (combine - combine_hi.astype(jnp.float32)).astype(jnp.bfloat16)
    stacked = jnp.concatenate([combine_hi, combine_lo], axis=1)
    stacked, outgoing = lax.optimization_barrier((stacked, outgoing))
    incoming = lax.all_to_all(outgoing, "expert", split_axis=0, concat_axis=0, tiled=True)
    partial_rows = expert_ffn(incoming, gate_proj, up_proj, down_proj)
    returned = lax.all_to_all(partial_rows, "expert", split_axis=0, concat_axis=0, tiled=True)
    both_parts = jnp.dot(
        stacked.T, returned.reshape(slot_count, model_width), preferred_element_type=jnp.float32
    )
    mixed_rows = both_parts[:group_size] + both_parts[group_size:]
    pieces = mixed_rows.astype(jnp.bfloat16).reshape(dp_count, own_rows, model_width)
    gathered = lax.all_to_all(pieces, "dp", split_axis=0, concat_axis=0, tiled=True)
    mixed = jnp.sum(gathered.astype(jnp.float32), axis=0).astype(jnp.bfloat16)
    return mixed[None]


def solution(mesh):
    placed = (
        P("expert", None, None),
        P(),
        P("expert", None, None),
        P("expert", None, None),
        P("expert", "dp", None),
        P("expert", "dp", None),
        P("expert", "dp", None),
    )
    return jax.shard_map(
        body, mesh=mesh, in_specs=placed, out_specs=P("expert", "dp", None), check_vma=False
    )
```

```python
import jax
import jax.numpy as jnp
from jax import lax
from jax.experimental import pallas as pl
from jax.experimental.pallas import tpu as pltpu
from jax.sharding import PartitionSpec as P


def ffn_block(x_ref, gate_ref, up_ref, down_hbm, out_ref, down_buf, down_sem):
    fetch = pltpu.make_async_copy(down_hbm.at[pl.program_id(0)], down_buf, down_sem)
    fetch.start()
    width = x_ref.shape[3]
    rows = x_ref[...].reshape(x_ref.shape[0] * x_ref.shape[2], width)
    contract = (((1,), (1,)), ((), ()))
    gate_act = lax.dot_general(rows, gate_ref[0], contract, preferred_element_type=jnp.float32)
    up_act = lax.dot_general(rows, up_ref[0], contract, preferred_element_type=jnp.float32)
    hidden = (gate_act / (1.0 + jnp.exp(-gate_act)) * up_act).astype(jnp.bfloat16)
    fetch.wait()
    partial = jnp.dot(hidden, down_buf[...], preferred_element_type=jnp.float32)
    out_ref[...] = partial.astype(out_ref.dtype).reshape(out_ref.shape)


def expert_ffn(incoming, gate_proj, up_proj, down_proj):
    sources, local_experts, capacity, width = incoming.shape
    hidden_width = gate_proj.shape[1]
    per_step = 32
    row_spec = pl.BlockSpec((per_step, 1, capacity, width), lambda j, b: (b, j, 0, 0))
    weight_spec = pl.BlockSpec((1, hidden_width, width), lambda j, b: (j, 0, 0))
    rows = sources * local_experts * capacity
    return pl.pallas_call(
        ffn_block,
        grid=(local_experts, sources // per_step),
        in_specs=[row_spec, weight_spec, weight_spec, pl.BlockSpec(memory_space=pl.ANY)],
        out_specs=row_spec,
        out_shape=jax.ShapeDtypeStruct(incoming.shape, jnp.bfloat16),
        scratch_shapes=[
            pltpu.VMEM((hidden_width, width), down_proj.dtype),
            pltpu.SemaphoreType.DMA(()),
        ],
        cost_estimate=pl.CostEstimate(
            flops=6 * rows * hidden_width * width,
            transcendentals=rows * hidden_width,
            bytes_accessed=4 * rows * width + 6 * local_experts * hidden_width * width,
        ),
    )(incoming, gate_proj, up_proj, down_proj)


def body(tokens, norm_gain, expert_ids, route_weights, gate_proj, up_proj, down_proj):
    dp_count = lax.axis_size("dp")
    expert_count = lax.axis_size("expert")
    local_experts = gate_proj.shape[0]
    model_width = tokens.shape[2]
    group_ids = expert_ids[0]
    group_weights = route_weights[0]
    group_size = group_ids.shape[0]
    own_rows = group_size // dp_count
    top_k = group_ids.shape[1]
    experts = local_experts * expert_count
    capacity = dp_count * (group_size * top_k // (experts * dp_count) + 1)
    slot_count = experts * capacity
    tok_float = tokens[0].astype(jnp.float32)
    inv_rms = lax.rsqrt(jnp.mean(tok_float * tok_float, axis=-1, keepdims=True) + 1e-06)
    group_rows = (tok_float * inv_rms * norm_gain).astype(jnp.bfloat16)
    expert_at = jnp.arange(experts, dtype=jnp.int32)[None, :]
    picks = jnp.zeros((group_size, experts), jnp.bool_)
    weight_of = jnp.zeros((group_size, experts), jnp.float32)
    for choice in range(top_k):
        named = group_ids[:, choice : choice + 1] == expert_at
        picks = picks | named
        weight_of = weight_of + jnp.where(named, group_weights[:, choice : choice + 1], 0.0)
    token_at = jnp.arange(group_size, dtype=jnp.int32)
    earlier = (token_at[:, None] > token_at[None, :]).astype(jnp.bfloat16)
    rank = jnp.dot(earlier, picks.astype(jnp.bfloat16), preferred_element_type=jnp.float32)
    place_hit = picks[:, :, None] & (
        rank.astype(jnp.int32)[:, :, None] == jnp.arange(capacity, dtype=jnp.int32)[None, None, :]
    )
    slot_hit = jnp.transpose(place_hit, (1, 2, 0)).reshape(slot_count, group_size)
    dispatch = slot_hit.astype(jnp.bfloat16)
    combine = jnp.where(
        slot_hit, jnp.repeat(weight_of.T, capacity, axis=0), 0.0
    )
    outgoing = jnp.dot(dispatch, group_rows, preferred_element_type=jnp.float32).astype(
        jnp.bfloat16
    )
    outgoing = outgoing.reshape(expert_count, local_experts, capacity, model_width)
    combine_hi = combine.astype(jnp.bfloat16)
    combine_lo = (combine - combine_hi.astype(jnp.float32)).astype(jnp.bfloat16)
    stacked = jnp.concatenate([combine_hi, combine_lo], axis=1)
    stacked, outgoing = lax.optimization_barrier((stacked, outgoing))
    incoming = lax.all_to_all(outgoing, "expert", split_axis=0, concat_axis=0, tiled=True)
    partial_rows = expert_ffn(incoming, gate_proj, up_proj, down_proj)
    returned = lax.all_to_all(partial_rows, "expert", split_axis=0, concat_axis=0, tiled=True)
    both_parts = jnp.dot(
        stacked.T, returned.reshape(slot_count, model_width), preferred_element_type=jnp.float32
    )
    mixed_rows = both_parts[:group_size] + both_parts[group_size:]
    pieces = mixed_rows.astype(jnp.bfloat16).reshape(dp_count, own_rows, model_width)
    gathered = lax.all_to_all(pieces, "dp", split_axis=0, concat_axis=0, tiled=True)
    mixed = jnp.sum(gathered.astype(jnp.float32), axis=0).astype(jnp.bfloat16)
    return mixed[None]


def solution(mesh):
    placed = (
        P("expert", None, None),
        P(),
        P("expert", None, None),
        P("expert", None, None),
        P("expert", "dp", None),
        P("expert", "dp", None),
        P("expert", "dp", None),
    )
    return jax.shard_map(
        body, mesh=mesh, in_specs=placed, out_specs=P("expert", "dp", None), check_vma=False
    )
```
